512 devices in a mesh: seq: 32 (over z, core), chan: 16 (over y, x).
Axes of the slice: x: 4, y: 4, z: 16, core: 2. Of those that a mesh axis runs over, the one named last changes fastest.
Arguments:
- features: bfloat16 [3, 65536, 4096], P(None, ('seq', 'chan')), may hold values from -6 to 6
- short_weight: float32 [3, 3, 4096], replicated, may hold values from -3.5 to 3.5
- decay_rate: float32 [16, 4096], P(None, 'chan'), as said below
- residue: float32 [16, 4096], P(None, 'chan'), may hold values from -1.5 to 1.5
- skip_gain: float32 [4096], P('chan'), may hold values from 0.5 to 1.5
Outputs:
- mixed: bfloat16 [65536, 4096], P(('seq', 'chan'))
The draws below stay inside these ranges and needn't reach their ends.
Inputs may be any that keep to these rules, and one draw needn't show every extreme that they name: `decay_rate`: every rate is positive and at most 1/30.
All inputs are finite; a program needn't handle non-finite values.
Results may differ from the reference program's by a relative error of at most 0.0075.
Values may be sent and summed in bfloat16 or wider, within the bound.
No kernel may reach another device: no remote copies, remote signals or barrier semaphores. Data moves between devices by JAX's collectives and lax.ppermute only.
A program may use at most 64 MiB of HBM per device.

```python
import math
import jax
import jax.numpy as jnp
from jax import lax

D = 4096
STATE = 16
SHORT = 3
TOKENS = 65536


def draw_decay_rate(key, part):
    first_key, second_key, third_key = jax.random.split(key, 3)
    share = 0.5
    slow_rates = jnp.exp(jax.random.uniform(second_key, (STATE, D), jnp.float32, math.log(0.2 / TOKENS), math.log(2.0 / TOKENS)))
    quick_rates = jnp.exp(jax.random.uniform(third_key, (STATE, D), jnp.float32, math.log(2.0 / TOKENS), math.log(1.0 / 30.0)))
    chosen = jax.random.uniform(first_key, (STATE, D), jnp.float32) < share
    return jnp.where(chosen, slow_rates, quick_rates)


def shard_levels(own_key, extent, cuts, smallest, high):
    def one(position, shards_of):
        draws = jax.random.uniform(jax.random.fold_in(jax.random.fold_in(own_key, 6), position), (shards_of,), jnp.float32, smallest / len(cuts), high / len(cuts))
        return jnp.repeat(jnp.exp(draws), extent[position] // shards_of).reshape((-1,) + (1,) * (len(extent) - position - 1))

    gain = one(*cuts[0])
    for cut in cuts[1:]:
        gain = gain * one(*cut)
    return gain


def normal_values(rng, extent, spread, reach, shards=(), held_as=jnp.bfloat16):
    result = spread * jax.random.normal(rng, extent, jnp.float32)
    if shards:
        result = result * shard_levels(rng, extent, shards, -0.22, 0.18)
    return jnp.clip(result, -reach, reach).astype(held_as)


def setup_inputs(seed: int = 0) -> dict:
    arg_keys = jax.random.split(jax.random.key(seed), 6)
    features = normal_values(arg_keys[0], (3, TOKENS, D), 1.0, 6.0, ((1, 512),))
    short_weight = normal_values(arg_keys[1], (3, SHORT, D), SHORT ** -0.5, 3.5, (), jnp.float32)
    decay_rate = draw_decay_rate(jax.random.fold_in(arg_keys[5], 71), 0)
    residue = normal_values(arg_keys[3], (STATE, D), 0.25, 1.5, ((1, 16),), jnp.float32)
    skip_gain = jnp.clip(0.5 + 1.0 * jax.random.uniform(arg_keys[4], (D,), jnp.float32) ** shard_levels(arg_keys[4], (D,), ((0, 16),), -0.2, 0.2), 0.5, 1.5)
    return dict(features=features, short_weight=short_weight, decay_rate=decay_rate, residue=residue, skip_gain=skip_gain)


block_len = 128

def short_filter(padded, weights, taps):
    length = padded.shape[1] - taps + 1
    total = jnp.zeros((padded.shape[0], length, padded.shape[2]), jnp.float32)
    for offset in range(taps):
        window = lax.slice_in_dim(padded, taps - 1 - offset, taps - 1 - offset + length, axis=1).astype(jnp.float32)
        total = total + weights[:, offset, :][:, None, :] * window
    return total

def modal_tables(decay_rate, scaled_residue, block):
    positions = jnp.arange(block).astype(jnp.float32)
    kernel = lax.optimization_barrier(jnp.sum(scaled_residue[:, None, :] * jnp.exp(-decay_rate[:, None, :] * positions[None, :, None]), axis=0))
    lag_index = (jnp.arange(block)[:, None] - jnp.arange(block)[None, :]).astype(jnp.int32)
    toeplitz = jnp.where((lag_index >= 0)[:, :, None], kernel[jnp.clip(lag_index, 0, block - 1)], jnp.zeros((), jnp.float32))
    ending = jnp.exp(-decay_rate[:, None, :] * (block - 1.0 - positions)[None, :, None])
    reading = scaled_residue[:, None, :] * jnp.exp(-decay_rate[:, None, :] * (positions + 1.0)[None, :, None])
    return (toeplitz, ending, reading)

def modal_conv(signal, decay_rate, tables, start_state, block):
    toeplitz, ending, reading = tables
    count = signal.shape[0] // block
    pieces = signal.reshape(count, block, signal.shape[1])
    inner = jnp.einsum('ijc,kjc->kic', toeplitz, pieces, precision=lax.Precision.HIGHEST)
    local_end = jnp.einsum('njc,kjc->knc', ending, pieces, precision=lax.Precision.HIGHEST)
    group_decay = jnp.exp(-decay_rate * block)

    def advance(state, piece):
        return (group_decay * state + piece, state)
    final, starts = lax.scan(advance, start_state, local_end)
    carried = jnp.einsum('nic,knc->kic', reading, starts, precision=lax.Precision.HIGHEST)
    return ((inner + carried).reshape(signal.shape), final)

def reference(features, short_weight, decay_rate, residue, skip_gain):
    width = math.gcd(D, 128)
    count = D // width
    block = math.gcd(TOKENS, block_len)

    def one_block(index):
        first = (index * width).astype(jnp.int32)
        streams = lax.dynamic_slice_in_dim(features, first, width, 2)
        weights = lax.dynamic_slice_in_dim(short_weight, first, width, 2)
        rates = lax.dynamic_slice_in_dim(decay_rate, first, width, 1)
        modes = lax.dynamic_slice_in_dim(residue, first, width, 1)
        skips = lax.dynamic_slice_in_dim(skip_gain, first, width, 0)
        padded = jnp.concatenate([jnp.zeros((3, SHORT - 1, width), features.dtype), streams], axis=1)
        filtered = lax.optimization_barrier(short_filter(padded, weights, SHORT).astype(jnp.bfloat16))
        product = lax.optimization_barrier((filtered[1].astype(jnp.float32) * filtered[2].astype(jnp.float32)).astype(jnp.bfloat16))
        signal = product.astype(jnp.float32)
        scaled = modes * jnp.sqrt(1.0 - jnp.exp(-2.0 * rates))
        tables = modal_tables(rates, scaled, block)
        longconv, unused_end = modal_conv(signal, rates, tables, jnp.zeros_like(rates), block)
        conv_out = lax.optimization_barrier((longconv + skips[None, :] * signal).astype(jnp.bfloat16))
        return (filtered[0].astype(jnp.float32) * conv_out.astype(jnp.float32)).astype(jnp.bfloat16)
    stacked = lax.map(one_block, jnp.arange(count, dtype=jnp.int32))
    return jnp.transpose(stacked, (1, 0, 2)).reshape(TOKENS, D)
```

```python
import math

import jax
import jax.numpy as jnp
from jax import lax
from jax.sharding import PartitionSpec as P

block_len = 64


def from_behind(block, axis, distance):
    devices = range(lax.axis_size(axis))
    route = [(i - distance, i) for i in devices if i - distance in devices]
    return lax.ppermute(block, axis, route)


def short_filter(padded, weights, taps):
    length = padded.shape[1] - taps + 1
    total = jnp.zeros((padded.shape[0], length, padded.shape[2]), jnp.float32)
    for offset in range(taps):
        window = lax.slice_in_dim(
            padded, taps - 1 - offset, taps - 1 - offset + length, axis=1
        ).astype(jnp.float32)
        total = total + weights[:, offset, :][:, None, :] * window
    return total


def modal_tables(decay_rate, scaled_residue, block):
    positions = jnp.arange(block).astype(jnp.float32)
    kernel = jnp.sum(
        scaled_residue[:, None, :] * jnp.exp(-decay_rate[:, None, :] * positions[None, :, None]),
        axis=0,
    )
    lag_index = jnp.arange(block)[:, None] - jnp.arange(block)[None, :]
    one_hot = (lag_index[:, :, None] == jnp.arange(block)[None, None, :]).astype(jnp.float32)
    toeplitz = jnp.dot(
        one_hot.reshape(block * block, block), kernel, precision=lax.Precision.HIGHEST
    ).reshape(block, block, kernel.shape[1])
    ending = jnp.exp(-decay_rate[:, None, :] * (block - 1.0 - positions)[None, :, None])
    reading = scaled_residue[:, None, :] * jnp.exp(
        -decay_rate[:, None, :] * (positions + 1.0)[None, :, None]
    )
    return (toeplitz, ending, reading)


def modal_conv(signal, decay_rate, tables, start_state, block):
    toeplitz, ending, reading = tables
    count = signal.shape[0] // block
    pieces = signal.reshape(count, block, signal.shape[1])
    inner = jnp.einsum("ijc,kjc->kic", toeplitz, pieces, precision=lax.Precision.HIGHEST)
    local_end = jnp.einsum("njc,kjc->knc", ending, pieces, precision=lax.Precision.HIGHEST)
    group_decay = jnp.exp(-decay_rate * block)

    def advance(state, piece):
        return (group_decay * state + piece, state)

    final, starts = lax.scan(advance, start_state, local_end)
    carried = jnp.einsum("nic,knc->kic", reading, starts, precision=lax.Precision.HIGHEST)
    return ((inner + carried).reshape(signal.shape), final)


def long_part(product, decay_rate, residue, skip_gain):
    signal = product.astype(jnp.float32)
    section = signal.shape[0]
    block = math.gcd(section, block_len)
    count = section // block
    scaled = residue * jnp.sqrt(1.0 - jnp.exp(-2.0 * decay_rate))
    tables = modal_tables(decay_rate, scaled, block)
    zero_state = jnp.zeros_like(decay_rate)
    longconv, end_state = modal_conv(signal, decay_rate, tables, zero_state, block)

    sections = lax.axis_size("seq")
    gathered = lax.all_gather(end_state, "seq")
    here = lax.axis_index("seq")
    earlier = jnp.arange(sections)
    lag = jnp.maximum(here - 1 - earlier, 0).astype(jnp.float32)
    weight = jnp.exp(-decay_rate[None, :, :] * (section * lag)[:, None, None])
    weight = jnp.where((earlier < here)[:, None, None], weight, 0.0)
    incoming = jnp.sum(weight * gathered, axis=0)
    block_starts = (jnp.arange(count).astype(jnp.float32) * block)[:, None, None]
    entering = jnp.exp(-decay_rate[None, :, :] * block_starts) * incoming[None, :, :]
    correction = jnp.einsum(
        "nic,knc->kic", tables[2], entering, precision=lax.Precision.HIGHEST
    ).reshape(signal.shape)
    return (longconv + correction + skip_gain[None, :] * signal).astype(jnp.bfloat16)


def local(features, short_weight, decay_rate, residue, skip_gain):
    taps = short_weight.shape[1]
    chan_width = decay_rate.shape[1]
    columns = lax.all_to_all(features, "chan", split_axis=2, concat_axis=1, tiled=True)
    border = from_behind(columns[:, columns.shape[1] - (taps - 1) :, :], "seq", 1)
    weights = lax.dynamic_slice_in_dim(
        short_weight, lax.axis_index("chan") * chan_width, chan_width, 2
    )
    padded = jnp.concatenate([border, columns], axis=1)
    filtered = lax.optimization_barrier(short_filter(padded, weights, taps).astype(jnp.bfloat16))
    product = lax.optimization_barrier(
        (filtered[1].astype(jnp.float32) * filtered[2].astype(jnp.float32)).astype(jnp.bfloat16)
    )
    conv_out = lax.optimization_barrier(long_part(product, decay_rate, residue, skip_gain))
    gated = (filtered[0].astype(jnp.float32) * conv_out.astype(jnp.float32)).astype(jnp.bfloat16)
    return lax.all_to_all(gated, "chan", split_axis=0, concat_axis=1, tiled=True)


def solution(mesh):
    return jax.shard_map(
        local,
        mesh=mesh,
        in_specs=(P(None, ("seq", "chan"), None), P(), P(None, "chan"), P(None, "chan"), P("chan")),
        out_specs=P(("seq", "chan"), None),
        check_vma=False,
    )
```

```python
import math

import jax
import jax.numpy as jnp
from jax import lax
from jax.sharding import PartitionSpec as P

block_len = 64


def from_behind(block, axis, distance):
    devices = range(lax.axis_size(axis))
    route = [(i - distance, i) for i in devices if i - distance in devices]
    return lax.ppermute(block, axis, route)


def short_filter(padded, weights, taps):
    length = padded.shape[1] - taps + 1
    total = jnp.zeros((padded.shape[0], length, padded.shape[2]), jnp.float32)
    for offset in range(taps):
        window = lax.slice_in_dim(
            padded, taps - 1 - offset, taps - 1 - offset + length, axis=1
        ).astype(jnp.float32)
        total = total + weights[:, offset, :][:, None, :] * window
    return total


def modal_tables(decay_rate, scaled_residue, block):
    positions = jnp.arange(block).astype(jnp.float32)
    kernel = jnp.sum(
        scaled_residue[:, None, :] * jnp.exp(-decay_rate[:, None, :] * positions[None, :, None]),
        axis=0,
    )
    lag_index = jnp.arange(block)[:, None] - jnp.arange(block)[None, :]
    one_hot = (lag_index[:, :, None] == jnp.arange(block)[None, None, :]).astype(jnp.float32)
    toeplitz = jnp.dot(
        one_hot.reshape(block * block, block), kernel, precision=lax.Precision.HIGHEST
    ).reshape(block, block, kernel.shape[1])
    ending = jnp.exp(-decay_rate[:, None, :] * (block - 1.0 - positions)[None, :, None])
    reading = scaled_residue[:, None, :] * jnp.exp(
        -decay_rate[:, None, :] * (positions + 1.0)[None, :, None]
    )
    return (toeplitz, ending, reading)


def shifted(values, distance):
    padding = jnp.zeros((distance,) + values.shape[1:], values.dtype)
    return jnp.concatenate([padding, values[: values.shape[0] - distance]], axis=0)


def long_part(product, decay_rate, residue, skip_gain):
    signal = product.astype(jnp.float32)
    section = signal.shape[0]
    block = math.gcd(section, block_len)
    count = section // block
    scaled = residue * jnp.sqrt(1.0 - jnp.exp(-2.0 * decay_rate))
    toeplitz, ending, reading = modal_tables(decay_rate, scaled, block)
    pieces = signal.reshape(count, block, signal.shape[1])
    local_end = jnp.einsum("njc,kjc->knc", ending, pieces, precision=lax.Precision.HIGHEST)
    starts = shifted(local_end, 1)
    step = 1
    while step < count:
        starts = starts + jnp.exp(-decay_rate * float(block * step)) * shifted(starts, step)
        step *= 2
    end_state = jnp.exp(-decay_rate * float(block)) * starts[count - 1] + local_end[count - 1]
    sections = lax.axis_size("seq")
    incoming = from_behind(end_state, "seq", 1)
    if sections > 2:
        incoming = incoming + jnp.exp(-decay_rate * float(section)) * from_behind(end_state, "seq", 2)
    step = 2
    while step < sections:
        incoming = incoming + jnp.exp(-decay_rate * float(section * step)) * from_behind(
            incoming, "seq", step
        )
        step *= 2
    inner = jnp.einsum("ijc,kjc->kic", toeplitz, pieces, precision=lax.Precision.HIGHEST)
    block_starts = (jnp.arange(count).astype(jnp.float32) * block)[:, None, None]
    starts = starts + jnp.exp(-decay_rate[None, :, :] * block_starts) * incoming[None, :, :]
    carried = jnp.einsum("nic,knc->kic", reading, starts, precision=lax.Precision.HIGHEST)
    longconv = (inner + carried).reshape(signal.shape)
    return (longconv + skip_gain[None, :] * signal).astype(jnp.bfloat16)


def local(features, short_weight, decay_rate, residue, skip_gain):
    taps = short_weight.shape[1]
    chan_width = decay_rate.shape[1]
    columns = lax.all_to_all(features, "chan", split_axis=2, concat_axis=1, tiled=True)
    border = from_behind(columns[:, columns.shape[1] - (taps - 1) :, :], "seq", 1)
    weights = lax.dynamic_slice_in_dim(
        short_weight, lax.axis_index("chan") * chan_width, chan_width, 2
    )
    padded = jnp.concatenate([border, columns], axis=1)
    filtered = lax.optimization_barrier(short_filter(padded, weights, taps).astype(jnp.bfloat16))
    product = lax.optimization_barrier(
        (filtered[1].astype(jnp.float32) * filtered[2].astype(jnp.float32)).astype(jnp.bfloat16)
    )
    conv_out = lax.optimization_barrier(long_part(product, decay_rate, residue, skip_gain))
    gated = (filtered[0].astype(jnp.float32) * conv_out.astype(jnp.float32)).astype(jnp.bfloat16)
    return lax.all_to_all(gated, "chan", split_axis=0, concat_axis=1, tiled=True)


def solution(mesh):
    return jax.shard_map(
        local,
        mesh=mesh,
        in_specs=(P(None, ("seq", "chan"), None), P(), P(None, "chan"), P(None, "chan"), P("chan")),
        out_specs=P(("seq", "chan"), None),
        check_vma=False,
    )
```

```python
import math

import jax
import jax.numpy as jnp
from jax import lax
from jax.sharding import PartitionSpec as P

block_len = 64


def from_behind(block, axis, distance):
    devices = range(lax.axis_size(axis))
    route = [(i - distance, i) for i in devices if i - distance in devices]
    return lax.ppermute(block, axis, route)


def short_filter(padded, weights, taps):
    length = padded.shape[1] - taps + 1
    total = jnp.zeros((padded.shape[0], length, padded.shape[2]), jnp.float32)
    for offset in range(taps):
        window = lax.slice_in_dim(
            padded, taps - 1 - offset, taps - 1 - offset + length, axis=1
        ).astype(jnp.float32)
        total = total + weights[:, offset, :][:, None, :] * window
    return total


def modal_tables(decay_rate, scaled_residue, block):
    positions = jnp.arange(block).astype(jnp.float32)
    kernel = jnp.sum(
        scaled_residue[:, None, :] * jnp.exp(-decay_rate[:, None, :] * positions[None, :, None]),
        axis=0,
    )
    lag_index = jnp.arange(block)[:, None] - jnp.arange(block)[None, :]
    one_hot = (lag_index[:, :, None] == jnp.arange(block)[None, None, :]).astype(jnp.float32)
    toeplitz = jnp.dot(
        one_hot.reshape(block * block, block), kernel, precision=lax.Precision.HIGHEST
    ).reshape(block, block, kernel.shape[1])
    ending = jnp.exp(-decay_rate[:, None, :] * (block - 1.0 - positions)[None, :, None])
    reading = scaled_residue[:, None, :] * jnp.exp(
        -decay_rate[:, None, :] * (positions + 1.0)[None, :, None]
    )
    return (toeplitz, ending, reading)


def channel_toeplitz(decay_rate, scaled_residue, block):
    positions = jnp.arange(block).astype(jnp.float32)
    kernel = jnp.sum(
        scaled_residue[:, :, None] * jnp.exp(-decay_rate[:, :, None] * positions[None, None, :]),
        axis=0,
    )
    lag_index = jnp.arange(block)[:, None] - jnp.arange(block)[None, :]
    one_hot = (jnp.arange(block)[:, None, None] == lag_index[None, :, :]).astype(jnp.float32)
    return jnp.dot(
        kernel, one_hot.reshape(block, block * block), precision=lax.Precision.HIGHEST
    ).reshape(kernel.shape[0], block, block)


def shifted(values, distance):
    padding = jnp.zeros((distance,) + values.shape[1:], values.dtype)
    return jnp.concatenate([padding, values[: values.shape[0] - distance]], axis=0)


def long_part(product, decay_rate, residue, skip_gain):
    signal = product.astype(jnp.float32)
    section = signal.shape[0]
    block = math.gcd(section, block_len)
    count = section // block
    scaled = residue * jnp.sqrt(1.0 - jnp.exp(-2.0 * decay_rate))
    positions = jnp.arange(block).astype(jnp.float32)
    ending = jnp.exp(-decay_rate[:, None, :] * (block - 1.0 - positions)[None, :, None])
    reading = scaled[:, None, :] * jnp.exp(-decay_rate[:, None, :] * (positions + 1.0)[None, :, None])
    pieces = signal.reshape(count, block, signal.shape[1])
    local_end = jnp.einsum("njc,kjc->knc", ending, pieces, precision=lax.Precision.HIGHEST)
    starts = shifted(local_end, 1)
    step = 1
    while step < count:
        starts = starts + jnp.exp(-decay_rate * float(block * step)) * shifted(starts, step)
        step *= 2
    end_state = jnp.exp(-decay_rate * float(block)) * starts[count - 1] + local_end[count - 1]

    def toeplitz_of(rates, modes):
        return modal_tables(rates, modes, block)[0]

    def inner_of(first, last):
        def work(toeplitz, chunk):
            return jnp.einsum("ijc,kjc->kic", toeplitz, chunk, precision=lax.Precision.HIGHEST)

        return work, first, last

    sections = lax.axis_size("seq")
    incoming = from_behind(end_state, "seq", 1)
    if sections > 2:
        incoming = incoming + jnp.exp(-decay_rate * float(section)) * from_behind(end_state, "seq", 2)
    slots = len([d for d in (2 ** i for i in range(1, sections.bit_length())) if d < sections])
    chunks = max(slots - 1, 1)
    splits = [count * i // chunks for i in range(chunks + 1)]
    toeplitz = None
    inner_parts = []
    step = 2
    slot = 0
    while step < sections:
        if slot == 0:
            incoming, rates, modes = lax.optimization_barrier((incoming, decay_rate, scaled))
            toeplitz = channel_toeplitz(rates, modes, block)
        else:
            first, last = splits[slot - 1], splits[slot]
            incoming, chunk = lax.optimization_barrier((incoming, pieces[first:last]))
            inner_parts.append(
                jnp.einsum("cij,kjc->kic", toeplitz, chunk, precision=lax.Precision.HIGHEST)
            )
        slot += 1
        incoming = incoming + jnp.exp(-decay_rate * float(section * step)) * from_behind(
            incoming, "seq", step
        )
        step *= 2
    if toeplitz is None:
        toeplitz = channel_toeplitz(decay_rate, scaled, block)
    done = sum(part.shape[0] for part in inner_parts)
    if done < count:
        inner_parts.append(
            jnp.einsum("cij,kjc->kic", toeplitz, pieces[done:], precision=lax.Precision.HIGHEST)
        )
    inner = jnp.concatenate(inner_parts, axis=0)
    block_starts = (jnp.arange(count).astype(jnp.float32) * block)[:, None, None]
    starts = starts + jnp.exp(-decay_rate[None, :, :] * block_starts) * incoming[None, :, :]
    carried = jnp.einsum("nic,knc->kic", reading, starts, precision=lax.Precision.HIGHEST)
    longconv = (inner + carried).reshape(signal.shape)
    return (longconv + skip_gain[None, :] * signal).astype(jnp.bfloat16)


def local(features, short_weight, decay_rate, residue, skip_gain):
    taps = short_weight.shape[1]
    chan_width = decay_rate.shape[1]
    columns = lax.all_to_all(features, "chan", split_axis=2, concat_axis=1, tiled=True)
    border = from_behind(columns[:, columns.shape[1] - (taps - 1) :, :], "seq", 1)
    weights = lax.dynamic_slice_in_dim(
        short_weight, lax.axis_index("chan") * chan_width, chan_width, 2
    )
    padded = jnp.concatenate([border, columns], axis=1)
    filtered = lax.optimization_barrier(short_filter(padded, weights, taps).astype(jnp.bfloat16))
    product = lax.optimization_barrier(
        (filtered[1].astype(jnp.float32) * filtered[2].astype(jnp.float32)).astype(jnp.bfloat16)
    )
    conv_out = lax.optimization_barrier(long_part(product, decay_rate, residue, skip_gain))
    gated = (filtered[0].astype(jnp.float32) * conv_out.astype(jnp.float32)).astype(jnp.bfloat16)
    return lax.all_to_all(gated, "chan", split_axis=0, concat_axis=1, tiled=True)


def solution(mesh):
    return jax.shard_map(
        local,
        mesh=mesh,
        in_specs=(P(None, ("seq", "chan"), None), P(), P(None, "chan"), P(None, "chan"), P("chan")),
        out_specs=P(("seq", "chan"), None),
        check_vma=False,
    )
```

```python
import math

import jax
import jax.numpy as jnp
from jax import lax
from jax.sharding import PartitionSpec as P

block_len = 64


def from_behind(block, axis, distance):
    devices = range(lax.axis_size(axis))
    route = [(i - distance, i) for i in devices if i - distance in devices]
    return lax.ppermute(block, axis, route)


def short_filter(padded, weights, taps):
    length = padded.shape[1] - taps + 1
    total = jnp.zeros((padded.shape[0], length, padded.shape[2]), jnp.float32)
    for offset in range(taps):
        window = lax.slice_in_dim(
            padded, taps - 1 - offset, taps - 1 - offset + length, axis=1
        ).astype(jnp.float32)
        total = total + weights[:, offset, :][:, None, :] * window
    return total


def modal_tables(decay_rate, scaled_residue, block):
    positions = jnp.arange(block).astype(jnp.float32)
    kernel = jnp.sum(
        scaled_residue[:, None, :] * jnp.exp(-decay_rate[:, None, :] * positions[None, :, None]),
        axis=0,
    )
    lag_index = jnp.arange(block)[:, None] - jnp.arange(block)[None, :]
    one_hot = (lag_index[:, :, None] == jnp.arange(block)[None, None, :]).astype(jnp.float32)
    toeplitz = jnp.dot(
        one_hot.reshape(block * block, block), kernel, precision=lax.Precision.HIGHEST
    ).reshape(block, block, kernel.shape[1])
    ending = jnp.exp(-decay_rate[:, None, :] * (block - 1.0 - positions)[None, :, None])
    reading = scaled_residue[:, None, :] * jnp.exp(
        -decay_rate[:, None, :] * (positions + 1.0)[None, :, None]
    )
    return (toeplitz, ending, reading)


def shifted(values, distance):
    padding = jnp.zeros((distance,) + values.shape[1:], values.dtype)
    return jnp.concatenate([padding, values[: values.shape[0] - distance]], axis=0)


def long_part(product, decay_rate, residue, skip_gain, passenger):
    signal = product.astype(jnp.float32)
    section = signal.shape[0]
    block = math.gcd(section, block_len)
    count = section // block
    scaled = residue * jnp.sqrt(1.0 - jnp.exp(-2.0 * decay_rate))
    toeplitz, ending, reading = modal_tables(decay_rate, scaled, block)
    pieces = signal.reshape(count, block, signal.shape[1])
    local_end = jnp.einsum("njc,kjc->knc", ending, pieces, precision=lax.Precision.HIGHEST)
    starts = shifted(local_end, 1)
    step = 1
    while step < count:
        starts = starts + jnp.exp(-decay_rate * float(block * step)) * shifted(starts, step)
        step *= 2
    end_state = jnp.exp(-decay_rate * float(block)) * starts[count - 1] + local_end[count - 1]
    end_state, passenger = lax.optimization_barrier((end_state, passenger))
    sections = lax.axis_size("seq")
    incoming = from_behind(end_state, "seq", 1)
    if sections > 2:
        incoming = incoming + jnp.exp(-decay_rate * float(section)) * from_behind(end_state, "seq", 2)
    step = 2
    while step < sections:
        incoming = incoming + jnp.exp(-decay_rate * float(section * step)) * from_behind(
            incoming, "seq", step
        )
        step *= 2
    inner = jnp.einsum("ijc,kjc->kic", toeplitz, pieces, precision=lax.Precision.HIGHEST)
    block_starts = (jnp.arange(count).astype(jnp.float32) * block)[:, None, None]
    starts = starts + jnp.exp(-decay_rate[None, :, :] * block_starts) * incoming[None, :, :]
    carried = jnp.einsum("nic,knc->kic", reading, starts, precision=lax.Precision.HIGHEST)
    longconv = (inner + carried).reshape(signal.shape)
    return (longconv + skip_gain[None, :] * signal).astype(jnp.bfloat16), passenger


def local(features, short_weight, decay_rate, residue, skip_gain):
    taps = short_weight.shape[1]
    chan_width = decay_rate.shape[1]
    weights = lax.dynamic_slice_in_dim(
        short_weight, lax.axis_index("chan") * chan_width, chan_width, 2
    )

    def arrive(streams):
        columns = lax.all_to_all(streams, "chan", split_axis=2, concat_axis=1, tiled=True)
        border = from_behind(columns[:, columns.shape[1] - (taps - 1) :, :], "seq", 1)
        return jnp.concatenate([border, columns], axis=1)

    keys_values = arrive(features[1:])
    keys_values, queries = lax.optimization_barrier((keys_values, features[:1]))
    queries = arrive(queries)
    gates = short_filter(keys_values, weights[1:], taps).astype(jnp.bfloat16)
    gates = lax.optimization_barrier(gates)
    product = lax.optimization_barrier(
        (gates[0].astype(jnp.float32) * gates[1].astype(jnp.float32)).astype(jnp.bfloat16)
    )
    conv_out, queries = lax.optimization_barrier(
        long_part(product, decay_rate, residue, skip_gain, queries)
    )
    query = short_filter(queries, weights[:1], taps).astype(jnp.bfloat16)[0]
    gated = (query.astype(jnp.float32) * conv_out.astype(jnp.float32)).astype(jnp.bfloat16)
    return lax.all_to_all(gated, "chan", split_axis=0, concat_axis=1, tiled=True)


def solution(mesh):
    return jax.shard_map(
        local,
        mesh=mesh,
        in_specs=(P(None, ("seq", "chan"), None), P(), P(None, "chan"), P(None, "chan"), P("chan")),
        out_specs=P(("seq", "chan"), None),
        check_vma=False,
    )
```

```python
import math

import jax
import jax.numpy as jnp
from jax import lax
from jax.sharding import PartitionSpec as P

block_len = 64


def from_behind(block, axis, distance):
    devices = range(lax.axis_size(axis))
    route = [(i - distance, i) for i in devices if i - distance in devices]
    return lax.ppermute(block, axis, route)


def short_filter(padded, weights, taps):
    length = padded.shape[1] - taps + 1
    total = jnp.zeros((padded.shape[0], length, padded.shape[2]), jnp.float32)
    for offset in range(taps):
        window = lax.slice_in_dim(
            padded, taps - 1 - offset, taps - 1 - offset + length, axis=1
        ).astype(jnp.float32)
        total = total + weights[:, offset, :][:, None, :] * window
    return total


def modal_tables(decay_rate, scaled_residue, block):
    positions = jnp.arange(block).astype(jnp.float32)
    kernel = jnp.sum(
        scaled_residue[:, None, :] * jnp.exp(-decay_rate[:, None, :] * positions[None, :, None]),
        axis=0,
    )
    lag_index = jnp.arange(block)[:, None] - jnp.arange(block)[None, :]
    one_hot = (lag_index[:, :, None] == jnp.arange(block)[None, None, :]).astype(jnp.float32)
    toeplitz = jnp.dot(
        one_hot.reshape(block * block, block), kernel, precision=lax.Precision.HIGHEST
    ).reshape(block, block, kernel.shape[1])
    ending = jnp.exp(-decay_rate[:, None, :] * (block - 1.0 - positions)[None, :, None])
    reading = scaled_residue[:, None, :] * jnp.exp(
        -decay_rate[:, None, :] * (positions + 1.0)[None, :, None]
    )
    return (toeplitz, ending, reading)


def shifted(values, distance):
    padding = jnp.zeros((distance,) + values.shape[1:], values.dtype)
    return jnp.concatenate([padding, values[: values.shape[0] - distance]], axis=0)


def long_part(product, decay_rate, residue, skip_gain, passenger):
    signal = product.astype(jnp.float32)
    section = signal.shape[0]
    block = math.gcd(section, block_len)
    count = section // block
    scaled = residue * jnp.sqrt(1.0 - jnp.exp(-2.0 * decay_rate))
    toeplitz, ending, reading = modal_tables(decay_rate, scaled, block)
    pieces = signal.reshape(count, block, signal.shape[1])
    local_end = jnp.einsum("njc,kjc->knc", ending, pieces, precision=lax.Precision.HIGHEST)
    starts = shifted(local_end, 1)
    step = 1
    while step < count:
        starts = starts + jnp.exp(-decay_rate * float(block * step)) * shifted(starts, step)
        step *= 2
    end_state = jnp.exp(-decay_rate * float(block)) * starts[count - 1] + local_end[count - 1]
    end_state, passenger = lax.optimization_barrier((end_state, passenger))
    sections = lax.axis_size("seq")
    incoming = from_behind(end_state, "seq", 1)
    if sections > 2:
        incoming = incoming + jnp.exp(-decay_rate * float(section)) * from_behind(end_state, "seq", 2)
    step = 2
    while step < sections:
        incoming = incoming + jnp.exp(-decay_rate * float(section * step)) * from_behind(
            incoming, "seq", step
        )
        step *= 2
    inner = jnp.einsum("ijc,kjc->kic", toeplitz, pieces, precision=lax.Precision.HIGHEST)
    block_starts = (jnp.arange(count).astype(jnp.float32) * block)[:, None, None]
    starts = starts + jnp.exp(-decay_rate[None, :, :] * block_starts) * incoming[None, :, :]
    carried = jnp.einsum("nic,knc->kic", reading, starts, precision=lax.Precision.HIGHEST)
    longconv = (inner + carried).reshape(signal.shape)
    return (longconv + skip_gain[None, :] * signal).astype(jnp.bfloat16), passenger


def local(features, short_weight, decay_rate, residue, skip_gain):
    taps = short_weight.shape[1]
    chan_width = decay_rate.shape[1]
    weights = lax.dynamic_slice_in_dim(
        short_weight, lax.axis_index("chan") * chan_width, chan_width, 2
    )

    def arrive(streams):
        columns = lax.all_to_all(streams, "chan", split_axis=2, concat_axis=1, tiled=True)
        border = from_behind(columns[:, columns.shape[1] - (taps - 1) :, :], "seq", 1)
        return jnp.concatenate([border, columns], axis=1)

    keys_values = arrive(features[1:])
    keys_values, queries = lax.optimization_barrier((keys_values, features[0]))
    queries = lax.all_to_all(queries, "chan", split_axis=1, concat_axis=0, tiled=True)
    queries = queries[None]
    border = from_behind(queries[:, queries.shape[1] - (taps - 1) :, :], "seq", 1)
    queries = jnp.concatenate([border, queries], axis=1)
    gates = short_filter(keys_values, weights[1:], taps).astype(jnp.bfloat16)
    gates = lax.optimization_barrier(gates)
    product = lax.optimization_barrier(
        (gates[0].astype(jnp.float32) * gates[1].astype(jnp.float32)).astype(jnp.bfloat16)
    )
    conv_out, queries = lax.optimization_barrier(
        long_part(product, decay_rate, residue, skip_gain, queries)
    )
    query = short_filter(queries, weights[:1], taps).astype(jnp.bfloat16)[0]
    gated = (query.astype(jnp.float32) * conv_out.astype(jnp.float32)).astype(jnp.bfloat16)
    return lax.all_to_all(gated, "chan", split_axis=0, concat_axis=1, tiled=True)


def solution(mesh):
    return jax.shard_map(
        local,
        mesh=mesh,
        in_specs=(P(None, ("seq", "chan"), None), P(), P(None, "chan"), P(None, "chan"), P("chan")),
        out_specs=P(("seq", "chan"), None),
        check_vma=False,
    )
```

```python
import math

import jax
import jax.numpy as jnp
from jax import lax
from jax.sharding import PartitionSpec as P

block_len = 64


def from_behind(block, axis, distance):
    devices = range(lax.axis_size(axis))
    route = [(i - distance, i) for i in devices if i - distance in devices]
    return lax.ppermute(block, axis, route)


def short_filter(padded, weights, taps):
    length = padded.shape[1] - taps + 1
    total = jnp.zeros((padded.shape[0], length, padded.shape[2]), jnp.float32)
    for offset in range(taps):
        window = lax.slice_in_dim(
            padded, taps - 1 - offset, taps - 1 - offset + length, axis=1
        ).astype(jnp.float32)
        total = total + weights[:, offset, :][:, None, :] * window
    return total


def modal_tables(decay_rate, scaled_residue, block):
    positions = jnp.arange(block).astype(jnp.float32)
    kernel = jnp.sum(
        scaled_residue[:, None, :] * jnp.exp(-decay_rate[:, None, :] * positions[None, :, None]),
        axis=0,
    )
    lag_index = jnp.arange(block)[:, None] - jnp.arange(block)[None, :]
    one_hot = (lag_index[:, :, None] == jnp.arange(block)[None, None, :]).astype(jnp.float32)
    toeplitz = jnp.dot(
        one_hot.reshape(block * block, block), kernel, precision=lax.Precision.HIGHEST
    ).reshape(block, block, kernel.shape[1])
    ending = jnp.exp(-decay_rate[:, None, :] * (block - 1.0 - positions)[None, :, None])
    reading = scaled_residue[:, None, :] * jnp.exp(
        -decay_rate[:, None, :] * (positions + 1.0)[None, :, None]
    )
    return (toeplitz, ending, reading)


def shifted(values, distance):
    padding = jnp.zeros((distance,) + values.shape[1:], values.dtype)
    return jnp.concatenate([padding, values[: values.shape[0] - distance]], axis=0)


def long_part(product, decay_rate, scaled, toeplitz, skip_gain, passenger):
    signal = product.astype(jnp.float32)
    section = signal.shape[0]
    block = math.gcd(section, block_len)
    count = section // block
    unused_toeplitz, ending, reading = modal_tables(decay_rate, scaled, block)
    pieces = signal.reshape(count, block, signal.shape[1])
    local_end = jnp.einsum("njc,kjc->knc", ending, pieces, precision=lax.Precision.HIGHEST)
    starts = shifted(local_end, 1)
    step = 1
    while step < count:
        starts = starts + jnp.exp(-decay_rate * float(block * step)) * shifted(starts, step)
        step *= 2
    end_state = jnp.exp(-decay_rate * float(block)) * starts[count - 1] + local_end[count - 1]
    end_state, passenger = lax.optimization_barrier((end_state, passenger))
    sections = lax.axis_size("seq")
    incoming = from_behind(end_state, "seq", 1)
    if sections > 2:
        incoming = incoming + jnp.exp(-decay_rate * float(section)) * from_behind(end_state, "seq", 2)
    step = 2
    while step < sections:
        incoming = incoming + jnp.exp(-decay_rate * float(section * step)) * from_behind(
            incoming, "seq", step
        )
        step *= 2
    inner = jnp.einsum("ijc,kjc->kic", toeplitz, pieces, precision=lax.Precision.HIGHEST)
    block_starts = (jnp.arange(count).astype(jnp.float32) * block)[:, None, None]
    starts = starts + jnp.exp(-decay_rate[None, :, :] * block_starts) * incoming[None, :, :]
    carried = jnp.einsum("nic,knc->kic", reading, starts, precision=lax.Precision.HIGHEST)
    longconv = (inner + carried).reshape(signal.shape)
    return (longconv + skip_gain[None, :] * signal).astype(jnp.bfloat16), passenger


def local(features, short_weight, decay_rate, residue, skip_gain):
    taps = short_weight.shape[1]
    chan_width = decay_rate.shape[1]
    weights = lax.dynamic_slice_in_dim(
        short_weight, lax.axis_index("chan") * chan_width, chan_width, 2
    )

    def arrive(streams):
        columns = lax.all_to_all(streams, "chan", split_axis=2, concat_axis=1, tiled=True)
        border = from_behind(columns[:, columns.shape[1] - (taps - 1) :, :], "seq", 1)
        return jnp.concatenate([border, columns], axis=1)

    scaled = residue * jnp.sqrt(1.0 - jnp.exp(-2.0 * decay_rate))
    section = features.shape[1] * lax.axis_size("chan")
    toeplitz = modal_tables(decay_rate, scaled, math.gcd(section, block_len))[0]
    keys_values = arrive(features[1:])
    keys_values, queries, toeplitz = lax.optimization_barrier((keys_values, features[0], toeplitz))
    queries = lax.all_to_all(queries, "chan", split_axis=1, concat_axis=0, tiled=True)
    queries = queries[None]
    border = from_behind(queries[:, queries.shape[1] - (taps - 1) :, :], "seq", 1)
    queries = jnp.concatenate([border, queries], axis=1)
    gates = short_filter(keys_values, weights[1:], taps).astype(jnp.bfloat16)
    gates = lax.optimization_barrier(gates)
    product = lax.optimization_barrier(
        (gates[0].astype(jnp.float32) * gates[1].astype(jnp.float32)).astype(jnp.bfloat16)
    )
    conv_out, queries = lax.optimization_barrier(
        long_part(product, decay_rate, scaled, toeplitz, skip_gain, queries)
    )
    query = short_filter(queries, weights[:1], taps).astype(jnp.bfloat16)[0]
    gated = (query.astype(jnp.float32) * conv_out.astype(jnp.float32)).astype(jnp.bfloat16)
    return lax.all_to_all(gated, "chan", split_axis=0, concat_axis=1, tiled=True)


def solution(mesh):
    return jax.shard_map(
        local,
        mesh=mesh,
        in_specs=(P(None, ("seq", "chan"), None), P(), P(None, "chan"), P(None, "chan"), P("chan")),
        out_specs=P(("seq", "chan"), None),
        check_vma=False,
    )
```

```python
import math

import jax
import jax.numpy as jnp
from jax import lax
from jax.sharding import PartitionSpec as P

block_len = 64


def from_behind(block, axis, distance):
    devices = range(lax.axis_size(axis))
    route = [(i - distance, i) for i in devices if i - distance in devices]
    return lax.ppermute(block, axis, route)


def short_filter(padded, weights, taps):
    length = padded.shape[1] - taps + 1
    total = jnp.zeros((padded.shape[0], length, padded.shape[2]), jnp.float32)
    for offset in range(taps):
        window = lax.slice_in_dim(
            padded, taps - 1 - offset, taps - 1 - offset + length, axis=1
        ).astype(jnp.float32)
        total = total + weights[:, offset, :][:, None, :] * window
    return total


def modal_tables(decay_rate, scaled_residue, block):
    positions = jnp.arange(block).astype(jnp.float32)
    kernel = jnp.sum(
        scaled_residue[:, None, :] * jnp.exp(-decay_rate[:, None, :] * positions[None, :, None]),
        axis=0,
    )
    lag_index = jnp.arange(block)[:, None] - jnp.arange(block)[None, :]
    one_hot = (lag_index[:, :, None] == jnp.arange(block)[None, None, :]).astype(jnp.float32)
    toeplitz = jnp.dot(
        one_hot.reshape(block * block, block), kernel, precision=lax.Precision.HIGHEST
    ).reshape(block, block, kernel.shape[1])
    ending = jnp.exp(-decay_rate[:, None, :] * (block - 1.0 - positions)[None, :, None])
    reading = scaled_residue[:, None, :] * jnp.exp(
        -decay_rate[:, None, :] * (positions + 1.0)[None, :, None]
    )
    return (toeplitz, ending, reading)


def shifted(values, distance):
    padding = jnp.zeros((distance,) + values.shape[1:], values.dtype)
    return jnp.concatenate([padding, values[: values.shape[0] - distance]], axis=0)


def long_part(product, decay_rate, scaled, toeplitz, skip_gain, passenger):
    signal = product.astype(jnp.float32)
    section = signal.shape[0]
    block = math.gcd(section, block_len)
    count = section // block
    unused_toeplitz, ending, reading = modal_tables(decay_rate, scaled, block)
    pieces = signal.reshape(count, block, signal.shape[1])
    local_end = jnp.einsum("njc,kjc->knc", ending, pieces, precision=lax.Precision.HIGHEST)
    starts = shifted(local_end, 1)
    step = 1
    while step < count:
        starts = starts + jnp.exp(-decay_rate * float(block * step)) * shifted(starts, step)
        step *= 2
    end_state = jnp.exp(-decay_rate * float(block)) * starts[count - 1] + local_end[count - 1]
    end_state, passenger = lax.optimization_barrier((end_state, passenger))
    sections = lax.axis_size("seq")
    here = lax.axis_index("seq")
    later = jnp.arange(sections)
    lag = jnp.maximum(later - 1 - here, 0).astype(jnp.float32)
    weight = jnp.exp(-decay_rate[None, :, :] * (section * lag)[:, None, None])
    weight = jnp.where((later > here)[:, None, None], weight, 0.0)
    incoming = lax.psum_scatter(weight * end_state[None], "seq", scatter_dimension=0, tiled=True)[0]
    inner = jnp.einsum("ijc,kjc->kic", toeplitz, pieces, precision=lax.Precision.HIGHEST)
    block_starts = (jnp.arange(count).astype(jnp.float32) * block)[:, None, None]
    starts = starts + jnp.exp(-decay_rate[None, :, :] * block_starts) * incoming[None, :, :]
    carried = jnp.einsum("nic,knc->kic", reading, starts, precision=lax.Precision.HIGHEST)
    longconv = (inner + carried).reshape(signal.shape)
    return (longconv + skip_gain[None, :] * signal).astype(jnp.bfloat16), passenger


def local(features, short_weight, decay_rate, residue, skip_gain):
    taps = short_weight.shape[1]
    chan_width = decay_rate.shape[1]
    weights = lax.dynamic_slice_in_dim(
        short_weight, lax.axis_index("chan") * chan_width, chan_width, 2
    )

    def arrive(streams):
        columns = lax.all_to_all(streams, "chan", split_axis=2, concat_axis=1, tiled=True)
        border = from_behind(columns[:, columns.shape[1] - (taps - 1) :, :], "seq", 1)
        return jnp.concatenate([border, columns], axis=1)

    scaled = residue * jnp.sqrt(1.0 - jnp.exp(-2.0 * decay_rate))
    section = features.shape[1] * lax.axis_size("chan")
    toeplitz = modal_tables(decay_rate, scaled, math.gcd(section, block_len))[0]
    keys_values = arrive(features[1:])
    keys_values, queries, toeplitz = lax.optimization_barrier((keys_values, features[0], toeplitz))
    queries = lax.all_to_all(queries, "chan", split_axis=1, concat_axis=0, tiled=True)
    queries = queries[None]
    border = from_behind(queries[:, queries.shape[1] - (taps - 1) :, :], "seq", 1)
    queries = jnp.concatenate([border, queries], axis=1)
    gates = short_filter(keys_values, weights[1:], taps).astype(jnp.bfloat16)
    gates = lax.optimization_barrier(gates)
    product = lax.optimization_barrier(
        (gates[0].astype(jnp.float32) * gates[1].astype(jnp.float32)).astype(jnp.bfloat16)
    )
    conv_out, queries = lax.optimization_barrier(
        long_part(product, decay_rate, scaled, toeplitz, skip_gain, queries)
    )
    query = short_filter(queries, weights[:1], taps).astype(jnp.bfloat16)[0]
    gated = (query.astype(jnp.float32) * conv_out.astype(jnp.float32)).astype(jnp.bfloat16)
    return lax.all_to_all(gated, "chan", split_axis=0, concat_axis=1, tiled=True)


def solution(mesh):
    return jax.shard_map(
        local,
        mesh=mesh,
        in_specs=(P(None, ("seq", "chan"), None), P(), P(None, "chan"), P(None, "chan"), P("chan")),
        out_specs=P(("seq", "chan"), None),
        check_vma=False,
    )
```

```python
import math

import jax
import jax.numpy as jnp
from jax import lax
from jax.sharding import PartitionSpec as P

block_len = 64


def from_behind(block, axis, distance):
    devices = range(lax.axis_size(axis))
    route = [(i - distance, i) for i in devices if i - distance in devices]
    return lax.ppermute(block, axis, route)


def short_filter(padded, weights, taps):
    length = padded.shape[1] - taps + 1
    total = jnp.zeros((padded.shape[0], length, padded.shape[2]), jnp.float32)
    for offset in range(taps):
        window = lax.slice_in_dim(
            padded, taps - 1 - offset, taps - 1 - offset + length, axis=1
        ).astype(jnp.float32)
        total = total + weights[:, offset, :][:, None, :] * window
    return total


def modal_tables(decay_rate, scaled_residue, block):
    positions = jnp.arange(block).astype(jnp.float32)
    kernel = jnp.sum(
        scaled_residue[:, None, :] * jnp.exp(-decay_rate[:, None, :] * positions[None, :, None]),
        axis=0,
    )
    lag_index = jnp.arange(block)[:, None] - jnp.arange(block)[None, :]
    one_hot = (lag_index[:, :, None] == jnp.arange(block)[None, None, :]).astype(jnp.float32)
    toeplitz = jnp.dot(
        one_hot.reshape(block * block, block), kernel, precision=lax.Precision.HIGHEST
    ).reshape(block, block, kernel.shape[1])
    ending = jnp.exp(-decay_rate[:, None, :] * (block - 1.0 - positions)[None, :, None])
    reading = scaled_residue[:, None, :] * jnp.exp(
        -decay_rate[:, None, :] * (positions + 1.0)[None, :, None]
    )
    return (toeplitz, ending, reading)


def shifted(values, distance):
    padding = jnp.zeros((distance,) + values.shape[1:], values.dtype)
    return jnp.concatenate([padding, values[: values.shape[0] - distance]], axis=0)


def long_part(product, decay_rate, scaled, toeplitz, skip_gain, passenger):
    signal = product.astype(jnp.float32)
    section = signal.shape[0]
    block = math.gcd(section, block_len)
    count = section // block
    unused_toeplitz, ending, reading = modal_tables(decay_rate, scaled, block)
    pieces = signal.reshape(count, block, signal.shape[1])
    local_end = jnp.einsum("njc,kjc->knc", ending, pieces, precision=lax.Precision.HIGHEST)
    starts = shifted(local_end, 1)
    step = 1
    while step < count:
        starts = starts + jnp.exp(-decay_rate * float(block * step)) * shifted(starts, step)
        step *= 2
    end_state = jnp.exp(-decay_rate * float(block)) * starts[count - 1] + local_end[count - 1]
    end_state, passenger = lax.optimization_barrier((end_state, passenger))
    sections = lax.axis_size("seq")
    radix = 4
    incoming = jnp.zeros_like(end_state)
    for distance in range(1, min(radix, sections - 1) + 1):
        weight = jnp.exp(-decay_rate * float(section * (distance - 1)))
        incoming = incoming + weight * from_behind(end_state, "seq", distance)
    span = radix
    while span < sections:
        total = incoming
        for multiple in range(1, radix):
            if span * multiple < sections:
                weight = jnp.exp(-decay_rate * float(section * span * multiple))
                total = total + weight * from_behind(incoming, "seq", span * multiple)
        incoming = total
        span *= radix
    inner = jnp.einsum("ijc,kjc->kic", toeplitz, pieces, precision=lax.Precision.HIGHEST)
    block_starts = (jnp.arange(count).astype(jnp.float32) * block)[:, None, None]
    starts = starts + jnp.exp(-decay_rate[None, :, :] * block_starts) * incoming[None, :, :]
    carried = jnp.einsum("nic,knc->kic", reading, starts, precision=lax.Precision.HIGHEST)
    longconv = (inner + carried).reshape(signal.shape)
    return (longconv + skip_gain[None, :] * signal).astype(jnp.bfloat16), passenger


def local(features, short_weight, decay_rate, residue, skip_gain):
    taps = short_weight.shape[1]
    chan_width = decay_rate.shape[1]
    weights = lax.dynamic_slice_in_dim(
        short_weight, lax.axis_index("chan") * chan_width, chan_width, 2
    )

    def arrive(streams):
        columns = lax.all_to_all(streams, "chan", split_axis=2, concat_axis=1, tiled=True)
        border = from_behind(columns[:, columns.shape[1] - (taps - 1) :, :], "seq", 1)
        return jnp.concatenate([border, columns], axis=1)

    scaled = residue * jnp.sqrt(1.0 - jnp.exp(-2.0 * decay_rate))
    section = features.shape[1] * lax.axis_size("chan")
    toeplitz = modal_tables(decay_rate, scaled, math.gcd(section, block_len))[0]
    keys_values = arrive(features[1:])
    keys_values, queries, toeplitz = lax.optimization_barrier((keys_values, features[0], toeplitz))
    queries = lax.all_to_all(queries, "chan", split_axis=1, concat_axis=0, tiled=True)
    queries = queries[None]
    border = from_behind(queries[:, queries.shape[1] - (taps - 1) :, :], "seq", 1)
    queries = jnp.concatenate([border, queries], axis=1)
    gates = short_filter(keys_values, weights[1:], taps).astype(jnp.bfloat16)
    gates = lax.optimization_barrier(gates)
    product = lax.optimization_barrier(
        (gates[0].astype(jnp.float32) * gates[1].astype(jnp.float32)).astype(jnp.bfloat16)
    )
    conv_out, queries = lax.optimization_barrier(
        long_part(product, decay_rate, scaled, toeplitz, skip_gain, queries)
    )
    query = short_filter(queries, weights[:1], taps).astype(jnp.bfloat16)[0]
    gated = (query.astype(jnp.float32) * conv_out.astype(jnp.float32)).astype(jnp.bfloat16)
    return lax.all_to_all(gated, "chan", split_axis=0, concat_axis=1, tiled=True)


def solution(mesh):
    return jax.shard_map(
        local,
        mesh=mesh,
        in_specs=(P(None, ("seq", "chan"), None), P(), P(None, "chan"), P(None, "chan"), P("chan")),
        out_specs=P(("seq", "chan"), None),
        check_vma=False,
    )
```

```python
import math

import jax
import jax.numpy as jnp
from jax import lax
from jax.sharding import PartitionSpec as P

block_len = 64


def from_behind(block, axis, distance):
    devices = range(lax.axis_size(axis))
    route = [(i - distance, i) for i in devices if i - distance in devices]
    return lax.ppermute(block, axis, route)


def short_filter(padded, weights, taps):
    length = padded.shape[1] - taps + 1
    total = jnp.zeros((padded.shape[0], length, padded.shape[2]), jnp.float32)
    for offset in range(taps):
        window = lax.slice_in_dim(
            padded, taps - 1 - offset, taps - 1 - offset + length, axis=1
        ).astype(jnp.float32)
        total = total + weights[:, offset, :][:, None, :] * window
    return total


def modal_tables(decay_rate, scaled_residue, block):
    positions = jnp.arange(block).astype(jnp.float32)
    kernel = jnp.sum(
        scaled_residue[:, None, :] * jnp.exp(-decay_rate[:, None, :] * positions[None, :, None]),
        axis=0,
    )
    lag_index = jnp.arange(block)[:, None] - jnp.arange(block)[None, :]
    one_hot = (lag_index[:, :, None] == jnp.arange(block)[None, None, :]).astype(jnp.float32)
    toeplitz = jnp.dot(
        one_hot.reshape(block * block, block), kernel, precision=lax.Precision.HIGHEST
    ).reshape(block, block, kernel.shape[1])
    ending = jnp.exp(-decay_rate[:, None, :] * (block - 1.0 - positions)[None, :, None])
    reading = scaled_residue[:, None, :] * jnp.exp(
        -decay_rate[:, None, :] * (positions + 1.0)[None, :, None]
    )
    return (toeplitz, ending, reading)


def shifted(values, distance):
    padding = jnp.zeros((distance,) + values.shape[1:], values.dtype)
    return jnp.concatenate([padding, values[: values.shape[0] - distance]], axis=0)


def long_part(product, decay_rate, scaled, toeplitz, skip_gain, passenger):
    signal = product.astype(jnp.float32)
    section = signal.shape[0]
    block = math.gcd(section, block_len)
    count = section // block
    unused_toeplitz, ending, reading = modal_tables(decay_rate, scaled, block)
    pieces = signal.reshape(count, block, signal.shape[1])
    local_end = jnp.einsum("njc,kjc->knc", ending, pieces, precision=lax.Precision.HIGHEST)
    starts = shifted(local_end, 1)
    step = 1
    while step < count:
        starts = starts + jnp.exp(-decay_rate * float(block * step)) * shifted(starts, step)
        step *= 2
    end_state = jnp.exp(-decay_rate * float(block)) * starts[count - 1] + local_end[count - 1]
    end_state, passenger = lax.optimization_barrier((end_state, passenger))
    sections = lax.axis_size("seq")
    radix = 4
    incoming = jnp.zeros_like(end_state)
    for distance in range(1, min(radix, sections - 1) + 1):
        weight = jnp.exp(-decay_rate * float(section * (distance - 1)))
        incoming = incoming + weight * from_behind(end_state, "seq", distance)
    span = radix
    while span < sections:
        total = incoming
        for multiple in range(1, radix):
            if span * multiple < sections:
                weight = jnp.exp(-decay_rate * float(section * span * multiple))
                total = total + weight * from_behind(incoming, "seq", span * multiple)
        incoming = total
        span *= radix
    block_starts = (jnp.arange(count).astype(jnp.float32) * block)[:, None, None]
    starts = starts + jnp.exp(-decay_rate[None, :, :] * block_starts) * incoming[None, :, :]
    operands = jnp.concatenate([pieces, starts], axis=1)
    longconv = jnp.einsum(
        "cij,kjc->kic", toeplitz, operands, precision=lax.Precision.HIGHEST
    ).reshape(signal.shape)
    return (longconv + skip_gain[None, :] * signal).astype(jnp.bfloat16), passenger


def local(features, short_weight, decay_rate, residue, skip_gain):
    taps = short_weight.shape[1]
    chan_width = decay_rate.shape[1]
    weights = lax.dynamic_slice_in_dim(
        short_weight, lax.axis_index("chan") * chan_width, chan_width, 2
    )

    def arrive(streams):
        columns = lax.all_to_all(streams, "chan", split_axis=2, concat_axis=1, tiled=True)
        border = from_behind(columns[:, columns.shape[1] - (taps - 1) :, :], "seq", 1)
        return jnp.concatenate([border, columns], axis=1)

    scaled = residue * jnp.sqrt(1.0 - jnp.exp(-2.0 * decay_rate))
    section = features.shape[1] * lax.axis_size("chan")
    toeplitz, unused_ending, reading = modal_tables(decay_rate, scaled, math.gcd(section, block_len))
    toeplitz = jnp.concatenate(
        [jnp.transpose(toeplitz, (2, 0, 1)), jnp.transpose(reading, (2, 1, 0))], axis=2
    )
    keys_values = arrive(features[1:])
    keys_values, queries, toeplitz = lax.optimization_barrier((keys_values, features[0], toeplitz))
    queries = lax.all_to_all(queries, "chan", split_axis=1, concat_axis=0, tiled=True)
    queries = queries[None]
    border = from_behind(queries[:, queries.shape[1] - (taps - 1) :, :], "seq", 1)
    queries = jnp.concatenate([border, queries], axis=1)
    gates = short_filter(keys_values, weights[1:], taps).astype(jnp.bfloat16)
    gates = lax.optimization_barrier(gates)
    product = lax.optimization_barrier(
        (gates[0].astype(jnp.float32) * gates[1].astype(jnp.float32)).astype(jnp.bfloat16)
    )
    conv_out, queries = lax.optimization_barrier(
        long_part(product, decay_rate, scaled, toeplitz, skip_gain, queries)
    )
    query = short_filter(queries, weights[:1], taps).astype(jnp.bfloat16)[0]
    gated = (query.astype(jnp.float32) * conv_out.astype(jnp.float32)).astype(jnp.bfloat16)
    return lax.all_to_all(gated, "chan", split_axis=0, concat_axis=1, tiled=True)


def solution(mesh):
    return jax.shard_map(
        local,
        mesh=mesh,
        in_specs=(P(None, ("seq", "chan"), None), P(), P(None, "chan"), P(None, "chan"), P("chan")),
        out_specs=P(("seq", "chan"), None),
        check_vma=False,
    )
```

```python
import math

import jax
import jax.numpy as jnp
from jax import lax
from jax.sharding import PartitionSpec as P

block_len = 32


def from_behind(block, axis, distance):
    devices = range(lax.axis_size(axis))
    route = [(i - distance, i) for i in devices if i - distance in devices]
    return lax.ppermute(block, axis, route)


def short_filter(padded, weights, taps):
    length = padded.shape[1] - taps + 1
    total = jnp.zeros((padded.shape[0], length, padded.shape[2]), jnp.float32)
    for offset in range(taps):
        window = lax.slice_in_dim(
            padded, taps - 1 - offset, taps - 1 - offset + length, axis=1
        ).astype(jnp.float32)
        total = total + weights[:, offset, :][:, None, :] * window
    return total


def modal_tables(decay_rate, scaled_residue, block):
    positions = jnp.arange(block).astype(jnp.float32)
    kernel = jnp.sum(
        scaled_residue[:, None, :] * jnp.exp(-decay_rate[:, None, :] * positions[None, :, None]),
        axis=0,
    )
    lag_index = jnp.arange(block)[:, None] - jnp.arange(block)[None, :]
    one_hot = (lag_index[:, :, None] == jnp.arange(block)[None, None, :]).astype(jnp.float32)
    toeplitz = jnp.dot(
        one_hot.reshape(block * block, block), kernel, precision=lax.Precision.HIGHEST
    ).reshape(block, block, kernel.shape[1])
    ending = jnp.exp(-decay_rate[:, None, :] * (block - 1.0 - positions)[None, :, None])
    reading = scaled_residue[:, None, :] * jnp.exp(
        -decay_rate[:, None, :] * (positions + 1.0)[None, :, None]
    )
    return (toeplitz, ending, reading)


def shifted(values, distance):
    padding = jnp.zeros((distance,) + values.shape[1:], values.dtype)
    return jnp.concatenate([padding, values[: values.shape[0] - distance]], axis=0)


def long_part(product, decay_rate, scaled, toeplitz, skip_gain, passenger):
    signal = product.astype(jnp.float32)
    section = signal.shape[0]
    block = math.gcd(section, block_len)
    count = section // block
    unused_toeplitz, ending, reading = modal_tables(decay_rate, scaled, block)
    pieces = signal.reshape(count, block, signal.shape[1])
    local_end = jnp.einsum("njc,kjc->knc", ending, pieces, precision=lax.Precision.HIGHEST)
    starts = shifted(local_end, 1)
    step = 1
    while step < count:
        starts = starts + jnp.exp(-decay_rate * float(block * step)) * shifted(starts, step)
        step *= 2
    end_state = jnp.exp(-decay_rate * float(block)) * starts[count - 1] + local_end[count - 1]
    end_state, passenger = lax.optimization_barrier((end_state, passenger))
    sections = lax.axis_size("seq")
    radix = 4
    incoming = jnp.zeros_like(end_state)
    for distance in range(1, min(radix, sections - 1) + 1):
        weight = jnp.exp(-decay_rate * float(section * (distance - 1)))
        incoming = incoming + weight * from_behind(end_state, "seq", distance)
    span = radix
    while span < sections:
        total = incoming
        for multiple in range(1, radix):
            if span * multiple < sections:
                weight = jnp.exp(-decay_rate * float(section * span * multiple))
                total = total + weight * from_behind(incoming, "seq", span * multiple)
        incoming = total
        span *= radix
    inner = jnp.einsum("ijc,kjc->kic", toeplitz, pieces, precision=lax.Precision.HIGHEST)
    block_starts = (jnp.arange(count).astype(jnp.float32) * block)[:, None, None]
    starts = starts + jnp.exp(-decay_rate[None, :, :] * block_starts) * incoming[None, :, :]
    carried = jnp.einsum("nic,knc->kic", reading, starts, precision=lax.Precision.HIGHEST)
    longconv = (inner + carried).reshape(signal.shape)
    return (longconv + skip_gain[None, :] * signal).astype(jnp.bfloat16), passenger


def local(features, short_weight, decay_rate, residue, skip_gain):
    taps = short_weight.shape[1]
    chan_width = decay_rate.shape[1]
    weights = lax.dynamic_slice_in_dim(
        short_weight, lax.axis_index("chan") * chan_width, chan_width, 2
    )

    def arrive(streams):
        columns = lax.all_to_all(streams, "chan", split_axis=2, concat_axis=1, tiled=True)
        border = from_behind(columns[:, columns.shape[1] - (taps - 1) :, :], "seq", 1)
        return jnp.concatenate([border, columns], axis=1)

    scaled = residue * jnp.sqrt(1.0 - jnp.exp(-2.0 * decay_rate))
    section = features.shape[1] * lax.axis_size("chan")
    toeplitz = modal_tables(decay_rate, scaled, math.gcd(section, block_len))[0]
    keys_values = arrive(features[1:])
    keys_values, queries, toeplitz = lax.optimization_barrier((keys_values, features[0], toeplitz))
    queries = lax.all_to_all(queries, "chan", split_axis=1, concat_axis=0, tiled=True)
    queries = queries[None]
    border = from_behind(queries[:, queries.shape[1] - (taps - 1) :, :], "seq", 1)
    queries = jnp.concatenate([border, queries], axis=1)
    gates = short_filter(keys_values, weights[1:], taps).astype(jnp.bfloat16)
    gates = lax.optimization_barrier(gates)
    product = lax.optimization_barrier(
        (gates[0].astype(jnp.float32) * gates[1].astype(jnp.float32)).astype(jnp.bfloat16)
    )
    conv_out, queries = lax.optimization_barrier(
        long_part(product, decay_rate, scaled, toeplitz, skip_gain, queries)
    )
    query = short_filter(queries, weights[:1], taps).astype(jnp.bfloat16)[0]
    gated = (query.astype(jnp.float32) * conv_out.astype(jnp.float32)).astype(jnp.bfloat16)
    return lax.all_to_all(gated, "chan", split_axis=0, concat_axis=1, tiled=True)


def solution(mesh):
    return jax.shard_map(
        local,
        mesh=mesh,
        in_specs=(P(None, ("seq", "chan"), None), P(), P(None, "chan"), P(None, "chan"), P("chan")),
        out_specs=P(("seq", "chan"), None),
        check_vma=False,
    )
```

```python
import math

import jax
import jax.numpy as jnp
from jax import lax
from jax.sharding import PartitionSpec as P

block_len = 16


def from_behind(block, axis, distance):
    devices = range(lax.axis_size(axis))
    route = [(i - distance, i) for i in devices if i - distance in devices]
    return lax.ppermute(block, axis, route)


def short_filter(padded, weights, taps):
    length = padded.shape[1] - taps + 1
    total = jnp.zeros((padded.shape[0], length, padded.shape[2]), jnp.float32)
    for offset in range(taps):
        window = lax.slice_in_dim(
            padded, taps - 1 - offset, taps - 1 - offset + length, axis=1
        ).astype(jnp.float32)
        total = total + weights[:, offset, :][:, None, :] * window
    return total


def modal_tables(decay_rate, scaled_residue, block):
    positions = jnp.arange(block).astype(jnp.float32)
    kernel = jnp.sum(
        scaled_residue[:, None, :] * jnp.exp(-decay_rate[:, None, :] * positions[None, :, None]),
        axis=0,
    )
    lag_index = jnp.arange(block)[:, None] - jnp.arange(block)[None, :]
    one_hot = (lag_index[:, :, None] == jnp.arange(block)[None, None, :]).astype(jnp.float32)
    toeplitz = jnp.dot(
        one_hot.reshape(block * block, block), kernel, precision=lax.Precision.HIGHEST
    ).reshape(block, block, kernel.shape[1])
    ending = jnp.exp(-decay_rate[:, None, :] * (block - 1.0 - positions)[None, :, None])
    reading = scaled_residue[:, None, :] * jnp.exp(
        -decay_rate[:, None, :] * (positions + 1.0)[None, :, None]
    )
    return (toeplitz, ending, reading)


def shifted(values, distance):
    padding = jnp.zeros((distance,) + values.shape[1:], values.dtype)
    return jnp.concatenate([padding, values[: values.shape[0] - distance]], axis=0)


def long_part(product, decay_rate, scaled, toeplitz, skip_gain, passenger):
    signal = product.astype(jnp.float32)
    section = signal.shape[0]
    block = math.gcd(section, block_len)
    count = section // block
    unused_toeplitz, ending, reading = modal_tables(decay_rate, scaled, block)
    pieces = signal.reshape(count, block, signal.shape[1])
    local_end = jnp.einsum("njc,kjc->knc", ending, pieces, precision=lax.Precision.HIGHEST)
    starts = shifted(local_end, 1)
    step = 1
    while step < count:
        starts = starts + jnp.exp(-decay_rate * float(block * step)) * shifted(starts, step)
        step *= 2
    end_state = jnp.exp(-decay_rate * float(block)) * starts[count - 1] + local_end[count - 1]
    end_state, passenger = lax.optimization_barrier((end_state, passenger))
    sections = lax.axis_size("seq")
    radix = 4
    incoming = jnp.zeros_like(end_state)
    for distance in range(1, min(radix, sections - 1) + 1):
        weight = jnp.exp(-decay_rate * float(section * (distance - 1)))
        incoming = incoming + weight * from_behind(end_state, "seq", distance)
    span = radix
    while span < sections:
        total = incoming
        for multiple in range(1, radix):
            if span * multiple < sections:
                weight = jnp.exp(-decay_rate * float(section * span * multiple))
                total = total + weight * from_behind(incoming, "seq", span * multiple)
        incoming = total
        span *= radix
    inner = jnp.einsum("ijc,kjc->kic", toeplitz, pieces, precision=lax.Precision.HIGHEST)
    block_starts = (jnp.arange(count).astype(jnp.float32) * block)[:, None, None]
    starts = starts + jnp.exp(-decay_rate[None, :, :] * block_starts) * incoming[None, :, :]
    carried = jnp.einsum("nic,knc->kic", reading, starts, precision=lax.Precision.HIGHEST)
    longconv = (inner + carried).reshape(signal.shape)
    return (longconv + skip_gain[None, :] * signal).astype(jnp.bfloat16), passenger


def local(features, short_weight, decay_rate, residue, skip_gain):
    taps = short_weight.shape[1]
    chan_width = decay_rate.shape[1]
    weights = lax.dynamic_slice_in_dim(
        short_weight, lax.axis_index("chan") * chan_width, chan_width, 2
    )

    def arrive(streams):
        columns = lax.all_to_all(streams, "chan", split_axis=2, concat_axis=1, tiled=True)
        border = from_behind(columns[:, columns.shape[1] - (taps - 1) :, :], "seq", 1)
        return jnp.concatenate([border, columns], axis=1)

    scaled = residue * jnp.sqrt(1.0 - jnp.exp(-2.0 * decay_rate))
    section = features.shape[1] * lax.axis_size("chan")
    toeplitz = modal_tables(decay_rate, scaled, math.gcd(section, block_len))[0]
    keys_values = arrive(features[1:])
    keys_values, queries, toeplitz = lax.optimization_barrier((keys_values, features[0], toeplitz))
    queries = lax.all_to_all(queries, "chan", split_axis=1, concat_axis=0, tiled=True)
    queries = queries[None]
    border = from_behind(queries[:, queries.shape[1] - (taps - 1) :, :], "seq", 1)
    queries = jnp.concatenate([border, queries], axis=1)
    gates = short_filter(keys_values, weights[1:], taps).astype(jnp.bfloat16)
    gates = lax.optimization_barrier(gates)
    product = lax.optimization_barrier(
        (gates[0].astype(jnp.float32) * gates[1].astype(jnp.float32)).astype(jnp.bfloat16)
    )
    conv_out, queries = lax.optimization_barrier(
        long_part(product, decay_rate, scaled, toeplitz, skip_gain, queries)
    )
    query = short_filter(queries, weights[:1], taps).astype(jnp.bfloat16)[0]
    gated = (query.astype(jnp.float32) * conv_out.astype(jnp.float32)).astype(jnp.bfloat16)
    return lax.all_to_all(gated, "chan", split_axis=0, concat_axis=1, tiled=True)


def solution(mesh):
    return jax.shard_map(
        local,
        mesh=mesh,
        in_specs=(P(None, ("seq", "chan"), None), P(), P(None, "chan"), P(None, "chan"), P("chan")),
        out_specs=P(("seq", "chan"), None),
        check_vma=False,
    )
```

```python
import math

import jax
import jax.numpy as jnp
from jax import lax
from jax.sharding import PartitionSpec as P

block_len = 8


def from_behind(block, axis, distance):
    devices = range(lax.axis_size(axis))
    route = [(i - distance, i) for i in devices if i - distance in devices]
    return lax.ppermute(block, axis, route)


def short_filter(padded, weights, taps):
    length = padded.shape[1] - taps + 1
    total = jnp.zeros((padded.shape[0], length, padded.shape[2]), jnp.float32)
    for offset in range(taps):
        window = lax.slice_in_dim(
            padded, taps - 1 - offset, taps - 1 - offset + length, axis=1
        ).astype(jnp.float32)
        total = total + weights[:, offset, :][:, None, :] * window
    return total


def modal_tables(decay_rate, scaled_residue, block):
    positions = jnp.arange(block).astype(jnp.float32)
    kernel = jnp.sum(
        scaled_residue[:, None, :] * jnp.exp(-decay_rate[:, None, :] * positions[None, :, None]),
        axis=0,
    )
    lag_index = jnp.arange(block)[:, None] - jnp.arange(block)[None, :]
    one_hot = (lag_index[:, :, None] == jnp.arange(block)[None, None, :]).astype(jnp.float32)
    toeplitz = jnp.dot(
        one_hot.reshape(block * block, block), kernel, precision=lax.Precision.HIGHEST
    ).reshape(block, block, kernel.shape[1])
    ending = jnp.exp(-decay_rate[:, None, :] * (block - 1.0 - positions)[None, :, None])
    reading = scaled_residue[:, None, :] * jnp.exp(
        -decay_rate[:, None, :] * (positions + 1.0)[None, :, None]
    )
    return (toeplitz, ending, reading)


def shifted(values, distance):
    padding = jnp.zeros((distance,) + values.shape[1:], values.dtype)
    return jnp.concatenate([padding, values[: values.shape[0] - distance]], axis=0)


def long_part(product, decay_rate, scaled, toeplitz, skip_gain, passenger):
    signal = product.astype(jnp.float32)
    section = signal.shape[0]
    block = math.gcd(section, block_len)
    count = section // block
    unused_toeplitz, ending, reading = modal_tables(decay_rate, scaled, block)
    pieces = signal.reshape(count, block, signal.shape[1])
    local_end = jnp.einsum("njc,kjc->knc", ending, pieces, precision=lax.Precision.HIGHEST)
    starts = shifted(local_end, 1)
    step = 1
    while step < count:
        starts = starts + jnp.exp(-decay_rate * float(block * step)) * shifted(starts, step)
        step *= 2
    end_state = jnp.exp(-decay_rate * float(block)) * starts[count - 1] + local_end[count - 1]
    end_state, passenger = lax.optimization_barrier((end_state, passenger))
    sections = lax.axis_size("seq")
    radix = 4
    incoming = jnp.zeros_like(end_state)
    for distance in range(1, min(radix, sections - 1) + 1):
        weight = jnp.exp(-decay_rate * float(section * (distance - 1)))
        incoming = incoming + weight * from_behind(end_state, "seq", distance)
    span = radix
    while span < sections:
        total = incoming
        for multiple in range(1, radix):
            if span * multiple < sections:
                weight = jnp.exp(-decay_rate * float(section * span * multiple))
                total = total + weight * from_behind(incoming, "seq", span * multiple)
        incoming = total
        span *= radix
    inner = jnp.einsum("ijc,kjc->kic", toeplitz, pieces, precision=lax.Precision.HIGHEST)
    block_starts = (jnp.arange(count).astype(jnp.float32) * block)[:, None, None]
    starts = starts + jnp.exp(-decay_rate[None, :, :] * block_starts) * incoming[None, :, :]
    carried = jnp.einsum("nic,knc->kic", reading, starts, precision=lax.Precision.HIGHEST)
    longconv = (inner + carried).reshape(signal.shape)
    return (longconv + skip_gain[None, :] * signal).astype(jnp.bfloat16), passenger


def local(features, short_weight, decay_rate, residue, skip_gain):
    taps = short_weight.shape[1]
    chan_width = decay_rate.shape[1]
    weights = lax.dynamic_slice_in_dim(
        short_weight, lax.axis_index("chan") * chan_width, chan_width, 2
    )

    def arrive(streams):
        columns = lax.all_to_all(streams, "chan", split_axis=2, concat_axis=1, tiled=True)
        border = from_behind(columns[:, columns.shape[1] - (taps - 1) :, :], "seq", 1)
        return jnp.concatenate([border, columns], axis=1)

    scaled = residue * jnp.sqrt(1.0 - jnp.exp(-2.0 * decay_rate))
    section = features.shape[1] * lax.axis_size("chan")
    toeplitz = modal_tables(decay_rate, scaled, math.gcd(section, block_len))[0]
    keys_values = arrive(features[1:])
    keys_values, queries, toeplitz = lax.optimization_barrier((keys_values, features[0], toeplitz))
    queries = lax.all_to_all(queries, "chan", split_axis=1, concat_axis=0, tiled=True)
    queries = queries[None]
    border = from_behind(queries[:, queries.shape[1] - (taps - 1) :, :], "seq", 1)
    queries = jnp.concatenate([border, queries], axis=1)
    gates = short_filter(keys_values, weights[1:], taps).astype(jnp.bfloat16)
    gates = lax.optimization_barrier(gates)
    product = lax.optimization_barrier(
        (gates[0].astype(jnp.float32) * gates[1].astype(jnp.float32)).astype(jnp.bfloat16)
    )
    conv_out, queries = lax.optimization_barrier(
        long_part(product, decay_rate, scaled, toeplitz, skip_gain, queries)
    )
    query = short_filter(queries, weights[:1], taps).astype(jnp.bfloat16)[0]
    gated = (query.astype(jnp.float32) * conv_out.astype(jnp.float32)).astype(jnp.bfloat16)
    return lax.all_to_all(gated, "chan", split_axis=0, concat_axis=1, tiled=True)


def solution(mesh):
    return jax.shard_map(
        local,
        mesh=mesh,
        in_specs=(P(None, ("seq", "chan"), None), P(), P(None, "chan"), P(None, "chan"), P("chan")),
        out_specs=P(("seq", "chan"), None),
        check_vma=False,
    )
```

```python
import math

import jax
import jax.numpy as jnp
from jax import lax
from jax.sharding import PartitionSpec as P

block_len = 16


def from_behind(block, axis, distance):
    devices = range(lax.axis_size(axis))
    route = [(i - distance, i) for i in devices if i - distance in devices]
    return lax.ppermute(block, axis, route)


def short_filter(padded, weights, taps):
    length = padded.shape[1] - taps + 1
    total = jnp.zeros((padded.shape[0], length, padded.shape[2]), jnp.float32)
    for offset in range(taps):
        window = lax.slice_in_dim(
            padded, taps - 1 - offset, taps - 1 - offset + length, axis=1
        ).astype(jnp.float32)
        total = total + weights[:, offset, :][:, None, :] * window
    return total


def modal_tables(decay_rate, scaled_residue, block):
    positions = jnp.arange(block).astype(jnp.float32)
    kernel = jnp.sum(
        scaled_residue[:, None, :] * jnp.exp(-decay_rate[:, None, :] * positions[None, :, None]),
        axis=0,
    )
    lag_index = jnp.arange(block)[:, None] - jnp.arange(block)[None, :]
    one_hot = (lag_index[:, :, None] == jnp.arange(block)[None, None, :]).astype(jnp.float32)
    toeplitz = jnp.dot(
        one_hot.reshape(block * block, block), kernel, precision=lax.Precision.HIGHEST
    ).reshape(block, block, kernel.shape[1])
    ending = jnp.exp(-decay_rate[:, None, :] * (block - 1.0 - positions)[None, :, None])
    reading = scaled_residue[:, None, :] * jnp.exp(
        -decay_rate[:, None, :] * (positions + 1.0)[None, :, None]
    )
    return (toeplitz, ending, reading)


def shifted(values, distance):
    padding = jnp.zeros((distance,) + values.shape[1:], values.dtype)
    return jnp.concatenate([padding, values[: values.shape[0] - distance]], axis=0)


def long_part(product, decay_rate, scaled, toeplitz, skip_gain, passenger):
    signal = product.astype(jnp.float32)
    section = signal.shape[0]
    block = math.gcd(section, block_len)
    count = section // block
    unused_toeplitz, ending, reading = modal_tables(decay_rate, scaled, block)
    pieces = signal.reshape(count, block, signal.shape[1])
    local_end = jnp.einsum("njc,kjc->knc", ending, pieces, precision=lax.Precision.HIGHEST)
    starts = shifted(local_end, 1)
    step = 1
    while step < count:
        starts = starts + jnp.exp(-decay_rate * float(block * step)) * shifted(starts, step)
        step *= 2
    end_state = jnp.exp(-decay_rate * float(block)) * starts[count - 1] + local_end[count - 1]
    end_state, passenger = lax.optimization_barrier((end_state, passenger))
    sections = lax.axis_size("seq")
    gathered = lax.all_gather(end_state, "seq")
    here = lax.axis_index("seq")
    earlier = jnp.arange(sections)
    lag = jnp.maximum(here - 1 - earlier, 0).astype(jnp.float32)
    weight = jnp.exp(-decay_rate[None, :, :] * (section * lag)[:, None, None])
    weight = jnp.where((earlier < here)[:, None, None], weight, 0.0)
    incoming = jnp.sum(weight * gathered, axis=0)
    inner = jnp.einsum("ijc,kjc->kic", toeplitz, pieces, precision=lax.Precision.HIGHEST)
    block_starts = (jnp.arange(count).astype(jnp.float32) * block)[:, None, None]
    starts = starts + jnp.exp(-decay_rate[None, :, :] * block_starts) * incoming[None, :, :]
    carried = jnp.einsum("nic,knc->kic", reading, starts, precision=lax.Precision.HIGHEST)
    longconv = (inner + carried).reshape(signal.shape)
    return (longconv + skip_gain[None, :] * signal).astype(jnp.bfloat16), passenger


def local(features, short_weight, decay_rate, residue, skip_gain):
    taps = short_weight.shape[1]
    chan_width = decay_rate.shape[1]
    weights = lax.dynamic_slice_in_dim(
        short_weight, lax.axis_index("chan") * chan_width, chan_width, 2
    )

    def arrive(streams):
        columns = lax.all_to_all(streams, "chan", split_axis=2, concat_axis=1, tiled=True)
        border = from_behind(columns[:, columns.shape[1] - (taps - 1) :, :], "seq", 1)
        return jnp.concatenate([border, columns], axis=1)

    scaled = residue * jnp.sqrt(1.0 - jnp.exp(-2.0 * decay_rate))
    section = features.shape[1] * lax.axis_size("chan")
    toeplitz = modal_tables(decay_rate, scaled, math.gcd(section, block_len))[0]
    keys_values = arrive(features[1:])
    keys_values, queries, toeplitz = lax.optimization_barrier((keys_values, features[0], toeplitz))
    queries = lax.all_to_all(queries, "chan", split_axis=1, concat_axis=0, tiled=True)
    queries = queries[None]
    border = from_behind(queries[:, queries.shape[1] - (taps - 1) :, :], "seq", 1)
    queries = jnp.concatenate([border, queries], axis=1)
    gates = short_filter(keys_values, weights[1:], taps).astype(jnp.bfloat16)
    gates = lax.optimization_barrier(gates)
    product = lax.optimization_barrier(
        (gates[0].astype(jnp.float32) * gates[1].astype(jnp.float32)).astype(jnp.bfloat16)
    )
    conv_out, queries = lax.optimization_barrier(
        long_part(product, decay_rate, scaled, toeplitz, skip_gain, queries)
    )
    query = short_filter(queries, weights[:1], taps).astype(jnp.bfloat16)[0]
    gated = (query.astype(jnp.float32) * conv_out.astype(jnp.float32)).astype(jnp.bfloat16)
    return lax.all_to_all(gated, "chan", split_axis=0, concat_axis=1, tiled=True)


def solution(mesh):
    return jax.shard_map(
        local,
        mesh=mesh,
        in_specs=(P(None, ("seq", "chan"), None), P(), P(None, "chan"), P(None, "chan"), P("chan")),
        out_specs=P(("seq", "chan"), None),
        check_vma=False,
    )
```

```python
import math

import jax
import jax.numpy as jnp
from jax import lax
from jax.sharding import PartitionSpec as P

block_len = 16


def from_behind(block, axis, distance):
    devices = range(lax.axis_size(axis))
    route = [(i - distance, i) for i in devices if i - distance in devices]
    return lax.ppermute(block, axis, route)


def short_filter(padded, weights, taps):
    length = padded.shape[1] - taps + 1
    total = jnp.zeros((padded.shape[0], length, padded.shape[2]), jnp.float32)
    for offset in range(taps):
        window = lax.slice_in_dim(
            padded, taps - 1 - offset, taps - 1 - offset + length, axis=1
        ).astype(jnp.float32)
        total = total + weights[:, offset, :][:, None, :] * window
    return total


def modal_tables(decay_rate, scaled_residue, block):
    positions = jnp.arange(block).astype(jnp.float32)
    kernel = jnp.sum(
        scaled_residue[:, None, :] * jnp.exp(-decay_rate[:, None, :] * positions[None, :, None]),
        axis=0,
    )
    lag_index = jnp.arange(block)[:, None] - jnp.arange(block)[None, :]
    one_hot = (lag_index[:, :, None] == jnp.arange(block)[None, None, :]).astype(jnp.float32)
    toeplitz = jnp.dot(
        one_hot.reshape(block * block, block), kernel, precision=lax.Precision.HIGHEST
    ).reshape(block, block, kernel.shape[1])
    ending = jnp.exp(-decay_rate[:, None, :] * (block - 1.0 - positions)[None, :, None])
    reading = scaled_residue[:, None, :] * jnp.exp(
        -decay_rate[:, None, :] * (positions + 1.0)[None, :, None]
    )
    return (toeplitz, ending, reading)


def shifted(values, distance):
    padding = jnp.zeros((distance,) + values.shape[1:], values.dtype)
    return jnp.concatenate([padding, values[: values.shape[0] - distance]], axis=0)


def long_part(product, decay_rate, scaled, toeplitz, skip_gain, passenger):
    signal = product.astype(jnp.float32)
    section = signal.shape[0]
    block = math.gcd(section, block_len)
    count = section // block
    unused_toeplitz, ending, reading = modal_tables(decay_rate, scaled, block)
    pieces = signal.reshape(count, block, signal.shape[1])
    local_end = jnp.einsum("njc,kjc->knc", ending, pieces, precision=lax.Precision.HIGHEST)
    starts = shifted(local_end, 1)
    step = 1
    while step < count:
        total = starts
        for multiple in range(1, 4):
            if step * multiple < count:
                weight = jnp.exp(-decay_rate * float(block * step * multiple))
                total = total + weight * shifted(starts, step * multiple)
        starts = total
        step *= 4
    end_state = jnp.exp(-decay_rate * float(block)) * starts[count - 1] + local_end[count - 1]
    end_state, passenger = lax.optimization_barrier((end_state, passenger))
    sections = lax.axis_size("seq")
    gathered = lax.all_gather(end_state, "seq")
    here = lax.axis_index("seq")
    earlier = jnp.arange(sections)
    lag = jnp.maximum(here - 1 - earlier, 0).astype(jnp.float32)
    weight = jnp.exp(-decay_rate[None, :, :] * (section * lag)[:, None, None])
    weight = jnp.where((earlier < here)[:, None, None], weight, 0.0)
    incoming = jnp.sum(weight * gathered, axis=0)
    inner = jnp.einsum("ijc,kjc->kic", toeplitz, pieces, precision=lax.Precision.HIGHEST)
    block_starts = (jnp.arange(count).astype(jnp.float32) * block)[:, None, None]
    starts = starts + jnp.exp(-decay_rate[None, :, :] * block_starts) * incoming[None, :, :]
    carried = jnp.einsum("nic,knc->kic", reading, starts, precision=lax.Precision.HIGHEST)
    longconv = (inner + carried).reshape(signal.shape)
    return (longconv + skip_gain[None, :] * signal).astype(jnp.bfloat16), passenger


def local(features, short_weight, decay_rate, residue, skip_gain):
    taps = short_weight.shape[1]
    chan_width = decay_rate.shape[1]
    weights = lax.dynamic_slice_in_dim(
        short_weight, lax.axis_index("chan") * chan_width, chan_width, 2
    )

    def arrive(streams):
        columns = lax.all_to_all(streams, "chan", split_axis=2, concat_axis=1, tiled=True)
        border = from_behind(columns[:, columns.shape[1] - (taps - 1) :, :], "seq", 1)
        return jnp.concatenate([border, columns], axis=1)

    scaled = residue * jnp.sqrt(1.0 - jnp.exp(-2.0 * decay_rate))
    section = features.shape[1] * lax.axis_size("chan")
    toeplitz = modal_tables(decay_rate, scaled, math.gcd(section, block_len))[0]
    keys_values = arrive(features[1:])
    keys_values, queries, toeplitz = lax.optimization_barrier((keys_values, features[0], toeplitz))
    queries = lax.all_to_all(queries, "chan", split_axis=1, concat_axis=0, tiled=True)
    queries = queries[None]
    border = from_behind(queries[:, queries.shape[1] - (taps - 1) :, :], "seq", 1)
    queries = jnp.concatenate([border, queries], axis=1)
    gates = short_filter(keys_values, weights[1:], taps).astype(jnp.bfloat16)
    gates = lax.optimization_barrier(gates)
    product = lax.optimization_barrier(
        (gates[0].astype(jnp.float32) * gates[1].astype(jnp.float32)).astype(jnp.bfloat16)
    )
    conv_out, queries = lax.optimization_barrier(
        long_part(product, decay_rate, scaled, toeplitz, skip_gain, queries)
    )
    query = short_filter(queries, weights[:1], taps).astype(jnp.bfloat16)[0]
    gated = (query.astype(jnp.float32) * conv_out.astype(jnp.float32)).astype(jnp.bfloat16)
    return lax.all_to_all(gated, "chan", split_axis=0, concat_axis=1, tiled=True)


def solution(mesh):
    return jax.shard_map(
        local,
        mesh=mesh,
        in_specs=(P(None, ("seq", "chan"), None), P(), P(None, "chan"), P(None, "chan"), P("chan")),
        out_specs=P(("seq", "chan"), None),
        check_vma=False,
    )
```

```python
import math

import jax
import jax.numpy as jnp
from jax import lax
from jax.sharding import PartitionSpec as P

block_len = 16


def from_behind(block, axis, distance):
    devices = range(lax.axis_size(axis))
    route = [(i - distance, i) for i in devices if i - distance in devices]
    return lax.ppermute(block, axis, route)


def short_filter(padded, weights, taps):
    length = padded.shape[1] - taps + 1
    total = jnp.zeros((padded.shape[0], length, padded.shape[2]), jnp.float32)
    for offset in range(taps):
        window = lax.slice_in_dim(
            padded, taps - 1 - offset, taps - 1 - offset + length, axis=1
        ).astype(jnp.float32)
        total = total + weights[:, offset, :][:, None, :] * window
    return total


def modal_tables(decay_rate, scaled_residue, block):
    positions = jnp.arange(block).astype(jnp.float32)
    kernel = jnp.sum(
        scaled_residue[:, None, :] * jnp.exp(-decay_rate[:, None, :] * positions[None, :, None]),
        axis=0,
    )
    lag_index = jnp.arange(block)[:, None] - jnp.arange(block)[None, :]
    one_hot = (lag_index[:, :, None] == jnp.arange(block)[None, None, :]).astype(jnp.float32)
    toeplitz = jnp.dot(
        one_hot.reshape(block * block, block), kernel, precision=lax.Precision.HIGHEST
    ).reshape(block, block, kernel.shape[1])
    ending = jnp.exp(-decay_rate[:, None, :] * (block - 1.0 - positions)[None, :, None])
    reading = scaled_residue[:, None, :] * jnp.exp(
        -decay_rate[:, None, :] * (positions + 1.0)[None, :, None]
    )
    return (toeplitz, ending, reading)


def shifted(values, distance):
    padding = jnp.zeros((distance,) + values.shape[1:], values.dtype)
    return jnp.concatenate([padding, values[: values.shape[0] - distance]], axis=0)


def long_part(product, decay_rate, scaled, toeplitz, skip_gain, passenger):
    signal = product.astype(jnp.float32)
    section = signal.shape[0]
    block = math.gcd(section, block_len)
    count = section // block
    unused_toeplitz, ending, reading = modal_tables(decay_rate, scaled, block)
    pieces = signal.reshape(count, block, signal.shape[1])
    local_end = jnp.einsum("njc,kjc->knc", ending, pieces, precision=lax.Precision.HIGHEST)
    starts = shifted(local_end, 1)
    step = 1
    while step < count:
        starts = starts + jnp.exp(-decay_rate * float(block * step)) * shifted(starts, step)
        step *= 2
    end_state = jnp.exp(-decay_rate * float(block)) * starts[count - 1] + local_end[count - 1]
    end_state, passenger = lax.optimization_barrier((end_state, passenger))
    sections = lax.axis_size("seq")
    gathered = lax.all_gather(end_state, "seq")
    here = lax.axis_index("seq")
    earlier = jnp.arange(sections)
    lag = jnp.maximum(here - 1 - earlier, 0).astype(jnp.float32)
    weight = jnp.exp(-decay_rate[None, :, :] * (section * lag)[:, None, None])
    weight = jnp.where((earlier < here)[:, None, None], weight, 0.0)
    incoming = jnp.sum(weight * gathered, axis=0)
    inner = jnp.einsum("ijc,kjc->kic", toeplitz, pieces, precision=lax.Precision.HIGHEST)
    block_starts = (jnp.arange(count).astype(jnp.float32) * block)[:, None, None]
    starts = starts + jnp.exp(-decay_rate[None, :, :] * block_starts) * incoming[None, :, :]
    carried = jnp.einsum("nic,knc->kic", reading, starts, precision=lax.Precision.HIGHEST)
    longconv = (inner + carried).reshape(signal.shape)
    return (longconv + skip_gain[None, :] * signal).astype(jnp.bfloat16), passenger


def local(features, short_weight, decay_rate, residue, skip_gain):
    taps = short_weight.shape[1]
    chan_width = decay_rate.shape[1]
    weights = lax.dynamic_slice_in_dim(
        short_weight, lax.axis_index("chan") * chan_width, chan_width, 2
    )

    def arrive(streams):
        columns = lax.all_to_all(streams, "chan", split_axis=2, concat_axis=1, tiled=True)
        border = from_behind(columns[:, columns.shape[1] - (taps - 1) :, :], "seq", 1)
        return jnp.concatenate([border, columns], axis=1)

    scaled = residue * jnp.sqrt(1.0 - jnp.exp(-2.0 * decay_rate))
    section = features.shape[1] * lax.axis_size("chan")
    toeplitz = modal_tables(decay_rate, scaled, math.gcd(section, block_len))[0]
    keys_values = arrive(features[1:])
    keys_values, queries, toeplitz = lax.optimization_barrier((keys_values, features[0], toeplitz))
    queries = lax.all_to_all(queries, "chan", split_axis=1, concat_axis=0, tiled=True)
    queries = queries[None]
    border = from_behind(queries[:, queries.shape[1] - (taps - 1) :, :], "seq", 1)
    queries = jnp.concatenate([border, queries], axis=1)
    gates = short_filter(keys_values, weights[1:], taps).astype(jnp.bfloat16)
    product = (gates[0].astype(jnp.float32) * gates[1].astype(jnp.float32)).astype(jnp.bfloat16)
    conv_out, queries = lax.optimization_barrier(
        long_part(product, decay_rate, scaled, toeplitz, skip_gain, queries)
    )
    query = short_filter(queries, weights[:1], taps).astype(jnp.bfloat16)[0]
    gated = (query.astype(jnp.float32) * conv_out.astype(jnp.float32)).astype(jnp.bfloat16)
    return lax.all_to_all(gated, "chan", split_axis=0, concat_axis=1, tiled=True)


def solution(mesh):
    return jax.shard_map(
        local,
        mesh=mesh,
        in_specs=(P(None, ("seq", "chan"), None), P(), P(None, "chan"), P(None, "chan"), P("chan")),
        out_specs=P(("seq", "chan"), None),
        check_vma=False,
    )
```
